256 devices in a mesh: rep: 32 (over z, y_hi, core), fsdp: 8 (over x, y_lo).
Axes of the slice: x: 4, y: 4 (y_hi: 2, y_lo: 2; y = y_hi * 2 + y_lo), z: 8, core: 2. Of those that a mesh axis runs over, the one named last changes fastest.
Arguments:
- hidden: bfloat16 [32768, 7168], P(('rep', 'fsdp')), may hold values from -6 to 6
- grad_out: bfloat16 [32768, 4096], P(('rep', 'fsdp')), may hold values from -24 to 24
- down_weight: bfloat16 [7168, 4096], P('fsdp'), may hold values from -0.0625 to 0.0625
- hash_tiles: bfloat16 [3, 32, 7168], P(None, None, 'fsdp'), may hold values from -1 to 1, as said below
- momentum: float32 [8, 3, 32, 4096], P('fsdp', None, None, 'rep'), may hold values from -6 to 6
- error: float32 [8, 3, 32, 4096], P('fsdp', None, None, 'rep'), may hold values from -6 to 6
Outputs:
- grad_hidden: bfloat16 [32768, 7168], P(('rep', 'fsdp'))
- update: float32 [7168, 4096], P('fsdp', 'rep')
- new_momentum: float32 [8, 3, 32, 4096], P('fsdp', None, None, 'rep')
- new_error: float32 [8, 3, 32, 4096], P('fsdp', None, None, 'rep')
The draws below stay inside these ranges and needn't reach their ends.
Inputs may be any that keep to these rules, and one draw needn't show every extreme that they name: `hash_tiles`: in every sketch row each hidden unit has exactly one nonzero entry, +1 or -1, in one of the 32 buckets; all other entries are 0.
All inputs are finite; a program needn't handle non-finite values.
Results may differ from the reference program's by a relative error of at most 0.0005.
Values may be sent and summed in bfloat16 or wider, within the bound.
No kernel may reach another device: no remote copies, remote signals or barrier semaphores. Data moves between devices by JAX's collectives and lax.ppermute only.
A program may use at most 128 MiB of HBM per device.

```python
import math
import jax
import jax.numpy as jnp
from jax import lax

D = 4096
FF = 7168
B = 32
ROWS = 3
TOKENS = 32768
N_FSDP = 8


def draw_hash_tiles(key, part):
    bucket_key, sign_key = jax.random.split(key)
    bucket_ids = jax.random.randint(bucket_key, (ROWS, FF), 0, B)
    sign_bits = jax.random.randint(sign_key, (ROWS, FF), 0, 2)
    signs = (2 * sign_bits - 1).astype(jnp.float32)
    levels = jnp.arange(B)
    dense = jnp.where(levels[None, :, None] == bucket_ids[:, None, :], signs[:, None, :], 0.0)
    return dense.astype(jnp.float32).astype(jnp.bfloat16)


def raised(result, own_key, source, target, shards_of, factor):
    owner, partner = [(jnp.arange(result.shape[axis_at]) // (result.shape[axis_at] // shards_of)).reshape([-1 if axis == axis_at else 1 for axis in range(result.ndim)]) for axis_at in (source, target)]
    chosen = jax.random.permutation(own_key, shards_of)[partner]
    strong = (owner == chosen) | (owner == (partner + shards_of // 2) % shards_of)
    return jnp.where(strong, factor * result, result)


def shard_levels(key, shape, cuts, low, largest):
    factor_of = 1.0
    for dim, blocks in cuts:
        draws = jax.random.uniform(jax.random.fold_in(jax.random.fold_in(key, 6), dim), (blocks,), jnp.float32, low / len(cuts), largest / len(cuts))
        factor_of = factor_of * jnp.repeat(jnp.exp(draws), shape[dim] // blocks).reshape((-1,) + (1,) * (len(shape) - 1 - dim))
    return factor_of


def noise(stream_key, shape, deviation, limit, cuts=(), held_as=jnp.bfloat16):
    gain = shard_levels(stream_key, shape, cuts, -0.22, 0.18) if cuts else 1.0
    array = jax.random.normal(stream_key, shape, jnp.float32) * deviation * gain
    return jnp.minimum(jnp.maximum(array, -limit), limit).astype(held_as)


def bell_draw_with(rng, dims, spread, limit, cuts, heavy, kind=jnp.bfloat16):
    entries = spread * jax.random.normal(rng, dims, jnp.float32)
    if cuts:
        entries = entries * shard_levels(rng, dims, cuts, -0.22, 0.18)
    return jnp.clip(raised(entries, jax.random.fold_in(rng, 3), *heavy), -limit, limit).astype(kind)


def setup_inputs(seed: int = 0) -> dict:
    keys = jax.random.split(jax.random.key(seed), 7)
    return {
        "hidden": noise(keys[0], (TOKENS, FF), 1.0, 6.0, ((0, 256),)),
        "grad_out": bell_draw_with(keys[1], (TOKENS, D), 1.0, 24.0, ((0, 256),), (0, 1, 256, 6.0)),
        "down_weight": noise(keys[2], (FF, D), FF ** -0.5, 0.0625, ((0, 8),)),
        "hash_tiles": draw_hash_tiles(jax.random.fold_in(keys[6], 71), 0),
        "momentum": noise(keys[4], (N_FSDP, ROWS, B, D), 1.0, 6.0, ((0, 8), (3, 32)), jnp.float32),
        "error": noise(keys[5], (N_FSDP, ROWS, B, D), 1.0, 6.0, ((0, 8), (3, 32)), jnp.float32),
    }


momentum_decay = 0.9
step_size = 0.5

def reference(hidden, grad_out, down_weight, hash_tiles, momentum, error):
    grad_hidden = jnp.dot(grad_out, down_weight.T, preferred_element_type=jnp.float32).astype(jnp.bfloat16)
    shard_rows = FF // N_FSDP
    table_scale = math.sqrt(B / (shard_rows * TOKENS))
    flat_hash = hash_tiles.reshape(ROWS * B, FF)
    grad_float = grad_out.astype(jnp.float32)
    moment_list = []
    error_list = []
    update_list = []
    for shard_index in range(N_FSDP):
        row_start = shard_index * shard_rows
        hash_tile = flat_hash[:, row_start:row_start + shard_rows]
        hidden_block = hidden[:, row_start:row_start + shard_rows]
        projected = jnp.dot(hash_tile, hidden_block.T, preferred_element_type=jnp.float32)
        sketch_table = jnp.dot(projected, grad_float, precision=lax.Precision.HIGHEST) * table_scale
        sketch_table = sketch_table.reshape(ROWS, B, D)
        moment_next = momentum_decay * momentum[shard_index] + sketch_table
        accumulated = error[shard_index] + step_size * moment_next
        hash_float = hash_tile.reshape(ROWS, B, shard_rows).astype(jnp.float32)
        shard_update = jnp.einsum('jbi,jbc->ic', hash_float, accumulated, precision=lax.Precision.HIGHEST) / ROWS
        error_next = accumulated - jnp.einsum('jbi,ic->jbc', hash_float, shard_update, precision=lax.Precision.HIGHEST)
        moment_list.append(moment_next)
        error_list.append(error_next)
        update_list.append(shard_update)
    update = jnp.concatenate(update_list, axis=0)
    return (grad_hidden, update, jnp.stack(moment_list), jnp.stack(error_list))
```

```python
import math

import jax
import jax.numpy as jnp
from jax import lax
from jax.sharding import PartitionSpec as P

momentum_decay = 0.9
step_size = 0.5


def split3(x):
    hi = lax.reduce_precision(x, exponent_bits=8, mantissa_bits=7)
    r1 = x - hi
    mid = lax.reduce_precision(r1, exponent_bits=8, mantissa_bits=7)
    lo = r1 - mid
    return jnp.stack([hi, mid, lo]).astype(jnp.bfloat16)


def on_device(hidden, grad_out, down_weight, hash_tiles, momentum, error):
    shards = lax.axis_size("fsdp")
    replicas = lax.axis_size("rep")
    tok_rows = grad_out.shape[0]
    model_width = grad_out.shape[1]
    shard_rows = down_weight.shape[0]
    rows_count = hash_tiles.shape[0]
    buckets = hash_tiles.shape[1]
    sketch_rows = rows_count * buckets
    columns = model_width // replicas
    total_tokens = tok_rows * shards * replicas
    table_scale = math.sqrt(buckets / (shard_rows * total_tokens))

    levels = jnp.arange(1, buckets + 1, dtype=jnp.float32)
    hash_float = hash_tiles.astype(jnp.float32)
    code = jnp.sum(hash_float * levels[None, :, None], axis=1).astype(jnp.bfloat16)
    all_code = lax.all_gather(code, "fsdp", axis=0, tiled=False).astype(jnp.float32)
    magnitude = jnp.abs(all_code)
    sign = jnp.where(all_code > 0, 1.0, -1.0)
    all_hash = jnp.where(
        magnitude[:, :, None, :] == levels[None, None, :, None], sign[:, :, None, :], 0.0
    ).astype(jnp.bfloat16)

    gathered = lax.all_gather(grad_out, "fsdp", axis=0, tiled=False)
    partial_grads = jnp.einsum(
        "ptd,hd->pth", gathered, down_weight, preferred_element_type=jnp.float32
    ).astype(jnp.bfloat16)
    grad_hidden = lax.all_to_all(
        partial_grads.reshape(shards * tok_rows, shard_rows), "fsdp",
        split_axis=0, concat_axis=1, tiled=True,
    )

    projected = jnp.einsum(
        "fki,tfi->fkt",
        all_hash.reshape(shards, sketch_rows, shard_rows),
        hidden.reshape(tok_rows, shards, shard_rows),
        preferred_element_type=jnp.float32,
    )
    received = lax.all_to_all(projected, "fsdp", split_axis=0, concat_axis=0, tiled=True)
    pieces = split3(received).transpose(1, 0, 2, 3).reshape(shards, 3 * sketch_rows, tok_rows)
    products = jnp.einsum(
        "pmt,ptrc->rmc",
        pieces,
        gathered.reshape(shards, tok_rows, replicas, columns),
        preferred_element_type=jnp.float32,
    ).reshape(replicas, 3, sketch_rows, columns)
    summed = products[:, 0] + products[:, 1] + products[:, 2]
    sketch_table = lax.psum_scatter(
        (summed * table_scale).reshape(replicas, rows_count, buckets, columns),
        "rep",
        scatter_dimension=0,
        tiled=True,
    )
    new_momentum = momentum_decay * momentum + sketch_table
    accumulated = error + step_size * new_momentum
    update = (
        jnp.einsum("jbi,jbc->ic", hash_float, accumulated[0], precision=lax.Precision.HIGHEST)
        / rows_count
    )
    encoded = jnp.einsum("jbi,ic->jbc", hash_float, update, precision=lax.Precision.HIGHEST)
    new_error = accumulated - encoded[None]
    return (grad_hidden, update, new_momentum, new_error)


def solution(mesh):
    return jax.shard_map(
        on_device,
        mesh=mesh,
        in_specs=(
            P(("rep", "fsdp"), None),
            P(("rep", "fsdp"), None),
            P("fsdp", None),
            P(None, None, "fsdp"),
            P("fsdp", None, None, "rep"),
            P("fsdp", None, None, "rep"),
        ),
        out_specs=(
            P(("rep", "fsdp"), None),
            P("fsdp", "rep"),
            P("fsdp", None, None, "rep"),
            P("fsdp", None, None, "rep"),
        ),
        check_vma=False,
    )
```

```python
import math

import jax
import jax.numpy as jnp
from jax import lax
from jax.sharding import PartitionSpec as P

momentum_decay = 0.9
step_size = 0.5


def split3(x):
    hi = lax.reduce_precision(x, exponent_bits=8, mantissa_bits=7)
    r1 = x - hi
    mid = lax.reduce_precision(r1, exponent_bits=8, mantissa_bits=7)
    lo = r1 - mid
    return jnp.stack([hi, mid, lo]).astype(jnp.bfloat16)


def on_device(hidden, grad_out, down_weight, hash_tiles, momentum, error):
    shards = lax.axis_size("fsdp")
    replicas = lax.axis_size("rep")
    tok_rows = grad_out.shape[0]
    model_width = grad_out.shape[1]
    shard_rows = down_weight.shape[0]
    rows_count = hash_tiles.shape[0]
    buckets = hash_tiles.shape[1]
    sketch_rows = rows_count * buckets
    columns = model_width // replicas
    total_tokens = tok_rows * shards * replicas
    table_scale = math.sqrt(buckets / (shard_rows * total_tokens))

    levels = jnp.arange(1, buckets + 1, dtype=jnp.float32)
    hash_float = hash_tiles.astype(jnp.float32)
    code = jnp.sum(hash_float * levels[None, :, None], axis=1).astype(jnp.bfloat16)
    all_code = lax.all_gather(code, "fsdp", axis=0, tiled=False).astype(jnp.float32)
    magnitude = jnp.abs(all_code)
    sign = jnp.where(all_code > 0, 1.0, -1.0)
    all_hash = jnp.where(
        magnitude[:, :, None, :] == levels[None, None, :, None], sign[:, :, None, :], 0.0
    ).astype(jnp.bfloat16)

    me = lax.axis_index("fsdp")

    def shifted(x, step):
        return lax.ppermute(x, "fsdp", [(j, (j + step) % shards) for j in range(shards)])

    projected = jnp.einsum(
        "fki,tfi->fkt",
        all_hash.reshape(shards, sketch_rows, shard_rows),
        hidden.reshape(tok_rows, shards, shard_rows),
        preferred_element_type=jnp.float32,
    )
    grad_hidden = jnp.zeros((tok_rows, shards * shard_rows), jnp.bfloat16)
    summed = jnp.zeros((3 * sketch_rows, model_width), jnp.float32)
    for step in range(shards):
        if step == 0:
            block = grad_out
            proj_block = lax.dynamic_index_in_dim(projected, me, keepdims=False)
        else:
            block = shifted(grad_out, step)
            proj_block = shifted(
                lax.dynamic_index_in_dim(projected, (me + step) % shards, keepdims=False), step
            )
        pieces = split3(proj_block).reshape(3 * sketch_rows, tok_rows)
        summed = summed + jnp.dot(pieces, block, preferred_element_type=jnp.float32)
        partial = jnp.einsum(
            "td,hd->th", block, down_weight, preferred_element_type=jnp.float32
        ).astype(jnp.bfloat16)
        if step > 0:
            partial = shifted(partial, shards - step)
        owner = (me + step) % shards
        grad_hidden = lax.dynamic_update_slice(grad_hidden, partial, (0, owner * shard_rows))
    summed = summed.reshape(3, sketch_rows, replicas, columns).transpose(2, 0, 1, 3)
    summed = summed[:, 0] + summed[:, 1] + summed[:, 2]
    sketch_table = lax.psum_scatter(
        (summed * table_scale).reshape(replicas, rows_count, buckets, columns),
        "rep",
        scatter_dimension=0,
        tiled=True,
    )
    new_momentum = momentum_decay * momentum + sketch_table
    accumulated = error + step_size * new_momentum
    update = (
        jnp.einsum("jbi,jbc->ic", hash_float, accumulated[0], precision=lax.Precision.HIGHEST)
        / rows_count
    )
    encoded = jnp.einsum("jbi,ic->jbc", hash_float, update, precision=lax.Precision.HIGHEST)
    new_error = accumulated - encoded[None]
    return (grad_hidden, update, new_momentum, new_error)


def solution(mesh):
    return jax.shard_map(
        on_device,
        mesh=mesh,
        in_specs=(
            P(("rep", "fsdp"), None),
            P(("rep", "fsdp"), None),
            P("fsdp", None),
            P(None, None, "fsdp"),
            P("fsdp", None, None, "rep"),
            P("fsdp", None, None, "rep"),
        ),
        out_specs=(
            P(("rep", "fsdp"), None),
            P("fsdp", "rep"),
            P("fsdp", None, None, "rep"),
            P("fsdp", None, None, "rep"),
        ),
        check_vma=False,
    )
```

```python
import math

import jax
import jax.numpy as jnp
from jax import lax
from jax.sharding import PartitionSpec as P

momentum_decay = 0.9
step_size = 0.5


def split3(x):
    hi = lax.reduce_precision(x, exponent_bits=8, mantissa_bits=7)
    r1 = x - hi
    mid = lax.reduce_precision(r1, exponent_bits=8, mantissa_bits=7)
    lo = r1 - mid
    return jnp.stack([hi, mid, lo]).astype(jnp.bfloat16)


def halving_scatter(blocks, replicas):
    me = lax.axis_index("rep")
    nbits = replicas.bit_length() - 1
    rest = blocks.shape[1:]
    data = blocks.reshape((2,) * nbits + rest)
    remaining = list(range(nbits - 1, -1, -1))
    for bit in (0, 2, 3, 4, 1)[:nbits] if nbits == 5 else range(nbits):
        axis = remaining.index(bit)
        mine = (me >> bit) & 1
        keep = lax.dynamic_index_in_dim(data, mine, axis=axis, keepdims=False)
        send = lax.dynamic_index_in_dim(data, 1 - mine, axis=axis, keepdims=False)
        pairs = [(j, j ^ (1 << bit)) for j in range(replicas)]
        data = keep + lax.ppermute(send, "rep", pairs)
        remaining.pop(axis)
    return data.reshape((1,) + rest)


def on_device(hidden, grad_out, down_weight, hash_tiles, momentum, error):
    shards = lax.axis_size("fsdp")
    replicas = lax.axis_size("rep")
    tok_rows = grad_out.shape[0]
    model_width = grad_out.shape[1]
    shard_rows = down_weight.shape[0]
    rows_count = hash_tiles.shape[0]
    buckets = hash_tiles.shape[1]
    sketch_rows = rows_count * buckets
    columns = model_width // replicas
    total_tokens = tok_rows * shards * replicas
    table_scale = math.sqrt(buckets / (shard_rows * total_tokens))

    levels = jnp.arange(1, buckets + 1, dtype=jnp.float32)
    hash_float = hash_tiles.astype(jnp.float32)
    code = jnp.sum(hash_float * levels[None, :, None], axis=1).astype(jnp.bfloat16)
    all_code = lax.all_gather(code, "fsdp", axis=0, tiled=False).astype(jnp.float32)
    magnitude = jnp.abs(all_code)
    sign = jnp.where(all_code > 0, 1.0, -1.0)
    all_hash = jnp.where(
        magnitude[:, :, None, :] == levels[None, None, :, None], sign[:, :, None, :], 0.0
    ).astype(jnp.bfloat16)

    all_hash, grad_out = lax.optimization_barrier((all_hash, grad_out))
    gathered = lax.all_gather(grad_out, "fsdp", axis=0, tiled=False)
    partial_grads = jnp.einsum(
        "ptd,hd->pth", gathered, down_weight, preferred_element_type=jnp.float32
    ).astype(jnp.bfloat16)
    grad_hidden = lax.all_to_all(
        partial_grads.reshape(shards * tok_rows, shard_rows), "fsdp",
        split_axis=0, concat_axis=1, tiled=True,
    )

    projected = jnp.einsum(
        "fki,tfi->fkt",
        all_hash.reshape(shards, sketch_rows, shard_rows),
        hidden.reshape(tok_rows, shards, shard_rows),
        preferred_element_type=jnp.float32,
    )
    received = lax.all_to_all(projected, "fsdp", split_axis=0, concat_axis=0, tiled=True)
    pieces = split3(received).transpose(1, 0, 2, 3).reshape(shards, 3 * sketch_rows, tok_rows)
    products = jnp.einsum(
        "pmt,ptrc->rmc",
        pieces,
        gathered.reshape(shards, tok_rows, replicas, columns),
        preferred_element_type=jnp.float32,
    ).reshape(replicas, 3, sketch_rows, columns)
    summed = products[:, 0] + products[:, 1] + products[:, 2]
    sketch_table = halving_scatter(
        (summed * table_scale).reshape(replicas, rows_count, buckets, columns), replicas
    )
    new_momentum = momentum_decay * momentum + sketch_table
    accumulated = error + step_size * new_momentum
    update = (
        jnp.einsum("jbi,jbc->ic", hash_float, accumulated[0], precision=lax.Precision.HIGHEST)
        / rows_count
    )
    encoded = jnp.einsum("jbi,ic->jbc", hash_float, update, precision=lax.Precision.HIGHEST)
    new_error = accumulated - encoded[None]
    return (grad_hidden, update, new_momentum, new_error)


def solution(mesh):
    return jax.shard_map(
        on_device,
        mesh=mesh,
        in_specs=(
            P(("rep", "fsdp"), None),
            P(("rep", "fsdp"), None),
            P("fsdp", None),
            P(None, None, "fsdp"),
            P("fsdp", None, None, "rep"),
            P("fsdp", None, None, "rep"),
        ),
        out_specs=(
            P(("rep", "fsdp"), None),
            P("fsdp", "rep"),
            P("fsdp", None, None, "rep"),
            P("fsdp", None, None, "rep"),
        ),
        check_vma=False,
    )
```

```python
import math

import jax
import jax.numpy as jnp
from jax import lax
from jax.sharding import PartitionSpec as P

momentum_decay = 0.9
step_size = 0.5


def split3(x):
    hi = lax.reduce_precision(x, exponent_bits=8, mantissa_bits=7)
    r1 = x - hi
    mid = lax.reduce_precision(r1, exponent_bits=8, mantissa_bits=7)
    lo = r1 - mid
    return jnp.stack([hi, mid, lo]).astype(jnp.bfloat16)


def halving_scatter(blocks, replicas):
    me = lax.axis_index("rep")
    nbits = replicas.bit_length() - 1
    rest = blocks.shape[1:]
    data = blocks.reshape((2,) * nbits + rest)
    remaining = list(range(nbits - 1, -1, -1))
    for bit in (0, 2, 3, 4, 1)[:nbits] if nbits == 5 else range(nbits):
        axis = remaining.index(bit)
        mine = (me >> bit) & 1
        keep = lax.dynamic_index_in_dim(data, mine, axis=axis, keepdims=False)
        send = lax.dynamic_index_in_dim(data, 1 - mine, axis=axis, keepdims=False)
        pairs = [(j, j ^ (1 << bit)) for j in range(replicas)]
        data = keep + lax.ppermute(send, "rep", pairs)
        remaining.pop(axis)
    return data.reshape((1,) + rest)


def on_device(hidden, grad_out, down_weight, hash_tiles, momentum, error):
    shards = lax.axis_size("fsdp")
    replicas = lax.axis_size("rep")
    tok_rows = grad_out.shape[0]
    model_width = grad_out.shape[1]
    shard_rows = down_weight.shape[0]
    rows_count = hash_tiles.shape[0]
    buckets = hash_tiles.shape[1]
    sketch_rows = rows_count * buckets
    columns = model_width // replicas
    total_tokens = tok_rows * shards * replicas
    table_scale = math.sqrt(buckets / (shard_rows * total_tokens))

    levels = jnp.arange(1, buckets + 1, dtype=jnp.float32)
    hash_float = hash_tiles.astype(jnp.float32)
    code = jnp.sum(hash_float * levels[None, :, None], axis=1).astype(jnp.bfloat16)
    all_code = lax.all_gather(code, "fsdp", axis=0, tiled=False).astype(jnp.float32)
    magnitude = jnp.abs(all_code)
    sign = jnp.where(all_code > 0, 1.0, -1.0)
    all_hash = jnp.where(
        magnitude[:, :, None, :] == levels[None, None, :, None], sign[:, :, None, :], 0.0
    ).astype(jnp.bfloat16)

    gathered = lax.all_gather(grad_out, "fsdp", axis=0, tiled=False)
    partial_grads = jnp.einsum(
        "ptd,hd->pth", gathered, down_weight, preferred_element_type=jnp.float32
    ).astype(jnp.bfloat16)
    grad_hidden = lax.all_to_all(
        partial_grads.reshape(shards * tok_rows, shard_rows), "fsdp",
        split_axis=0, concat_axis=1, tiled=True,
    )

    projected = jnp.einsum(
        "fki,tfi->fkt",
        all_hash.reshape(shards, sketch_rows, shard_rows),
        hidden.reshape(tok_rows, shards, shard_rows),
        preferred_element_type=jnp.float32,
    )
    received = lax.all_to_all(projected, "fsdp", split_axis=0, concat_axis=0, tiled=True)
    pieces = split3(received).transpose(0, 2, 1, 3).reshape(3 * sketch_rows, shards * tok_rows)
    products = jnp.dot(
        pieces, gathered.reshape(shards * tok_rows, model_width), preferred_element_type=jnp.float32
    ).reshape(3, sketch_rows, replicas, columns)
    summed = (products[0] + products[1] + products[2]).transpose(1, 0, 2)
    sketch_table = halving_scatter(
        (summed * table_scale).reshape(replicas, rows_count, buckets, columns), replicas
    )
    new_momentum = momentum_decay * momentum + sketch_table
    accumulated = error + step_size * new_momentum
    update = (
        jnp.einsum("jbi,jbc->ic", hash_float, accumulated[0], precision=lax.Precision.HIGHEST)
        / rows_count
    )
    encoded = jnp.einsum("jbi,ic->jbc", hash_float, update, precision=lax.Precision.HIGHEST)
    new_error = accumulated - encoded[None]
    return (grad_hidden, update, new_momentum, new_error)


def solution(mesh):
    return jax.shard_map(
        on_device,
        mesh=mesh,
        in_specs=(
            P(("rep", "fsdp"), None),
            P(("rep", "fsdp"), None),
            P("fsdp", None),
            P(None, None, "fsdp"),
            P("fsdp", None, None, "rep"),
            P("fsdp", None, None, "rep"),
        ),
        out_specs=(
            P(("rep", "fsdp"), None),
            P("fsdp", "rep"),
            P("fsdp", None, None, "rep"),
            P("fsdp", None, None, "rep"),
        ),
        check_vma=False,
    )
```

```python
import math

import jax
import jax.numpy as jnp
from jax import lax
from jax.sharding import PartitionSpec as P

momentum_decay = 0.9
step_size = 0.5


def split3(x):
    hi = lax.reduce_precision(x, exponent_bits=8, mantissa_bits=7)
    r1 = x - hi
    mid = lax.reduce_precision(r1, exponent_bits=8, mantissa_bits=7)
    lo = r1 - mid
    return jnp.stack([hi, mid, lo]).astype(jnp.bfloat16)


def halving_scatter(blocks, replicas):
    me = lax.axis_index("rep")
    nbits = replicas.bit_length() - 1
    rest = blocks.shape[1:]
    data = blocks.reshape((2,) * nbits + rest)
    remaining = list(range(nbits - 1, -1, -1))
    for bit in (0, 2, 3, 4, 1)[:nbits] if nbits == 5 else range(nbits):
        axis = remaining.index(bit)
        mine = (me >> bit) & 1
        keep = lax.dynamic_index_in_dim(data, mine, axis=axis, keepdims=False)
        send = lax.dynamic_index_in_dim(data, 1 - mine, axis=axis, keepdims=False)
        pairs = [(j, j ^ (1 << bit)) for j in range(replicas)]
        data = keep + lax.ppermute(send, "rep", pairs)
        remaining.pop(axis)
    return data.reshape((1,) + rest)


def on_device(hidden, grad_out, down_weight, hash_tiles, momentum, error):
    shards = lax.axis_size("fsdp")
    replicas = lax.axis_size("rep")
    tok_rows = grad_out.shape[0]
    model_width = grad_out.shape[1]
    shard_rows = down_weight.shape[0]
    rows_count = hash_tiles.shape[0]
    buckets = hash_tiles.shape[1]
    sketch_rows = rows_count * buckets
    columns = model_width // replicas
    total_tokens = tok_rows * shards * replicas
    table_scale = math.sqrt(buckets / (shard_rows * total_tokens))

    levels = jnp.arange(1, buckets + 1, dtype=jnp.float32)
    hash_float = hash_tiles.astype(jnp.float32)
    code = jnp.sum(hash_float * levels[None, :, None], axis=1).astype(jnp.bfloat16)
    all_code = lax.all_gather(code, "fsdp", axis=0, tiled=False).astype(jnp.float32)
    magnitude = jnp.abs(all_code)
    sign = jnp.where(all_code > 0, 1.0, -1.0)
    all_hash = jnp.where(
        magnitude[:, :, None, :] == levels[None, None, :, None], sign[:, :, None, :], 0.0
    ).astype(jnp.bfloat16)

    gathered = lax.all_gather(grad_out, "fsdp", axis=0, tiled=False)
    partial_grads = jnp.einsum(
        "ptd,hd->tph", gathered, down_weight, preferred_element_type=jnp.float32
    ).astype(jnp.bfloat16)
    grad_hidden = lax.all_to_all(
        partial_grads, "fsdp", split_axis=1, concat_axis=1, tiled=True
    ).reshape(tok_rows, shards * shard_rows)

    projected = jnp.einsum(
        "fki,tfi->fkt",
        all_hash.reshape(shards, sketch_rows, shard_rows),
        hidden.reshape(tok_rows, shards, shard_rows),
        preferred_element_type=jnp.float32,
    )
    received = lax.all_to_all(projected, "fsdp", split_axis=0, concat_axis=0, tiled=True)
    pieces = split3(received).transpose(0, 2, 1, 3).reshape(3 * sketch_rows, shards * tok_rows)
    products = jnp.dot(
        pieces, gathered.reshape(shards * tok_rows, model_width), preferred_element_type=jnp.float32
    ).reshape(3, sketch_rows, replicas, columns)
    summed = (products[0] + products[1] + products[2]).transpose(1, 0, 2)
    arrived = lax.all_to_all(
        (summed * table_scale).reshape(replicas, rows_count, buckets, columns),
        "rep", split_axis=0, concat_axis=0, tiled=True,
    )
    sketch_table = jnp.sum(arrived, axis=0, keepdims=True)
    new_momentum = momentum_decay * momentum + sketch_table
    accumulated = error + step_size * new_momentum
    update = (
        jnp.einsum("jbi,jbc->ic", hash_float, accumulated[0], precision=lax.Precision.HIGHEST)
        / rows_count
    )
    encoded = jnp.einsum("jbi,ic->jbc", hash_float, update, precision=lax.Precision.HIGHEST)
    new_error = accumulated - encoded[None]
    return (grad_hidden, update, new_momentum, new_error)


def solution(mesh):
    return jax.shard_map(
        on_device,
        mesh=mesh,
        in_specs=(
            P(("rep", "fsdp"), None),
            P(("rep", "fsdp"), None),
            P("fsdp", None),
            P(None, None, "fsdp"),
            P("fsdp", None, None, "rep"),
            P("fsdp", None, None, "rep"),
        ),
        out_specs=(
            P(("rep", "fsdp"), None),
            P("fsdp", "rep"),
            P("fsdp", None, None, "rep"),
            P("fsdp", None, None, "rep"),
        ),
        check_vma=False,
    )
```

```python
import math

import jax
import jax.numpy as jnp
from jax import lax
from jax.sharding import PartitionSpec as P

momentum_decay = 0.9
step_size = 0.5


def split3(x):
    hi = lax.reduce_precision(x, exponent_bits=8, mantissa_bits=7)
    r1 = x - hi
    mid = lax.reduce_precision(r1, exponent_bits=8, mantissa_bits=7)
    lo = r1 - mid
    return jnp.stack([hi, mid, lo]).astype(jnp.bfloat16)


def halving_scatter(blocks, replicas):
    me = lax.axis_index("rep")
    nbits = replicas.bit_length() - 1
    rest = blocks.shape[1:]
    data = blocks.reshape((2,) * nbits + rest)
    remaining = list(range(nbits - 1, -1, -1))
    for bit in (0, 2, 3, 4, 1)[:nbits] if nbits == 5 else range(nbits):
        axis = remaining.index(bit)
        mine = (me >> bit) & 1
        keep = lax.dynamic_index_in_dim(data, mine, axis=axis, keepdims=False)
        send = lax.dynamic_index_in_dim(data, 1 - mine, axis=axis, keepdims=False)
        pairs = [(j, j ^ (1 << bit)) for j in range(replicas)]
        data = keep + lax.ppermute(send, "rep", pairs)
        remaining.pop(axis)
    return data.reshape((1,) + rest)


def on_device(hidden, grad_out, down_weight, hash_tiles, momentum, error):
    shards = lax.axis_size("fsdp")
    replicas = lax.axis_size("rep")
    tok_rows = grad_out.shape[0]
    model_width = grad_out.shape[1]
    shard_rows = down_weight.shape[0]
    rows_count = hash_tiles.shape[0]
    buckets = hash_tiles.shape[1]
    sketch_rows = rows_count * buckets
    columns = model_width // replicas
    total_tokens = tok_rows * shards * replicas
    table_scale = math.sqrt(buckets / (shard_rows * total_tokens))

    hash_float = hash_tiles.astype(jnp.float32)

    outgoing = jnp.concatenate(
        [
            jnp.broadcast_to(grad_out[None], (shards, tok_rows, model_width)),
            hidden.reshape(tok_rows, shards, shard_rows).transpose(1, 0, 2),
        ],
        axis=2,
    )
    arrived = lax.all_to_all(outgoing, "fsdp", split_axis=0, concat_axis=0, tiled=True)
    gathered = arrived[:, :, :model_width]
    hidden_cols = arrived[:, :, model_width:]
    partial_grads = jnp.einsum(
        "ptd,hd->pth", gathered, down_weight, preferred_element_type=jnp.float32
    ).astype(jnp.bfloat16)
    grad_hidden = lax.all_to_all(
        partial_grads.reshape(shards * tok_rows, shard_rows), "fsdp",
        split_axis=0, concat_axis=1, tiled=True,
    )

    projected = jnp.einsum(
        "ki,pti->kpt",
        hash_tiles.reshape(sketch_rows, shard_rows),
        hidden_cols,
        preferred_element_type=jnp.float32,
    ).reshape(sketch_rows, shards * tok_rows)
    pieces = split3(projected).reshape(3 * sketch_rows, shards * tok_rows)
    products = jnp.dot(
        pieces, gathered.reshape(shards * tok_rows, model_width), preferred_element_type=jnp.float32
    ).reshape(3, sketch_rows, replicas, columns)
    summed = (products[0] + products[1] + products[2]).transpose(1, 0, 2)
    sketch_table = halving_scatter(
        (summed * table_scale).reshape(replicas, rows_count, buckets, columns), replicas
    )
    new_momentum = momentum_decay * momentum + sketch_table
    accumulated = error + step_size * new_momentum
    update = (
        jnp.einsum("jbi,jbc->ic", hash_float, accumulated[0], precision=lax.Precision.HIGHEST)
        / rows_count
    )
    encoded = jnp.einsum("jbi,ic->jbc", hash_float, update, precision=lax.Precision.HIGHEST)
    new_error = accumulated - encoded[None]
    return (grad_hidden, update, new_momentum, new_error)


def solution(mesh):
    return jax.shard_map(
        on_device,
        mesh=mesh,
        in_specs=(
            P(("rep", "fsdp"), None),
            P(("rep", "fsdp"), None),
            P("fsdp", None),
            P(None, None, "fsdp"),
            P("fsdp", None, None, "rep"),
            P("fsdp", None, None, "rep"),
        ),
        out_specs=(
            P(("rep", "fsdp"), None),
            P("fsdp", "rep"),
            P("fsdp", None, None, "rep"),
            P("fsdp", None, None, "rep"),
        ),
        check_vma=False,
    )
```

```python
import math

import jax
import jax.numpy as jnp
from jax import lax
from jax.sharding import PartitionSpec as P

momentum_decay = 0.9
step_size = 0.5


def split3(x):
    hi = lax.reduce_precision(x, exponent_bits=8, mantissa_bits=7)
    r1 = x - hi
    mid = lax.reduce_precision(r1, exponent_bits=8, mantissa_bits=7)
    lo = r1 - mid
    return jnp.stack([hi, mid, lo]).astype(jnp.bfloat16)


def grouped_scatter(blocks):
    me = lax.axis_index("rep")
    replicas = blocks.shape[0]
    inner = 4
    outer = replicas // inner
    rest = blocks.shape[1:]
    data = blocks.reshape((outer, inner) + rest)
    low = me % inner
    kept = lax.dynamic_index_in_dim(data, low, axis=1, keepdims=False)
    for mask in range(1, inner):
        send = lax.dynamic_index_in_dim(data, low ^ mask, axis=1, keepdims=False)
        kept = kept + lax.ppermute(send, "rep", [(j, j ^ mask) for j in range(replicas)])
    high = me // inner
    total = lax.dynamic_index_in_dim(kept, high, axis=0, keepdims=False)
    for mask in range(1, outer):
        send = lax.dynamic_index_in_dim(kept, high ^ mask, axis=0, keepdims=False)
        total = total + lax.ppermute(send, "rep", [(j, j ^ (mask * inner)) for j in range(replicas)])
    return total[None]


def on_device(hidden, grad_out, down_weight, hash_tiles, momentum, error):
    shards = lax.axis_size("fsdp")
    replicas = lax.axis_size("rep")
    tok_rows = grad_out.shape[0]
    model_width = grad_out.shape[1]
    shard_rows = down_weight.shape[0]
    rows_count = hash_tiles.shape[0]
    buckets = hash_tiles.shape[1]
    sketch_rows = rows_count * buckets
    columns = model_width // replicas
    total_tokens = tok_rows * shards * replicas
    table_scale = math.sqrt(buckets / (shard_rows * total_tokens))

    hash_float = hash_tiles.astype(jnp.float32)

    outgoing = jnp.concatenate(
        [
            jnp.broadcast_to(grad_out[None], (shards, tok_rows, model_width)),
            hidden.reshape(tok_rows, shards, shard_rows).transpose(1, 0, 2),
        ],
        axis=2,
    )
    arrived = lax.all_to_all(outgoing, "fsdp", split_axis=0, concat_axis=0, tiled=True)
    gathered = arrived[:, :, :model_width]
    hidden_cols = arrived[:, :, model_width:]
    partial_grads = jnp.einsum(
        "ptd,hd->pth", gathered, down_weight, preferred_element_type=jnp.float32
    ).astype(jnp.bfloat16)
    grad_hidden = lax.all_to_all(
        partial_grads.reshape(shards * tok_rows, shard_rows), "fsdp",
        split_axis=0, concat_axis=1, tiled=True,
    )

    projected = jnp.einsum(
        "ki,pti->kpt",
        hash_tiles.reshape(sketch_rows, shard_rows),
        hidden_cols,
        preferred_element_type=jnp.float32,
    ).reshape(sketch_rows, shards * tok_rows)
    pieces = split3(projected).reshape(3 * sketch_rows, shards * tok_rows)
    products = jnp.dot(
        pieces, gathered.reshape(shards * tok_rows, model_width), preferred_element_type=jnp.float32
    ).reshape(3, sketch_rows, replicas, columns)
    summed = (products[0] + products[1] + products[2]).transpose(1, 0, 2)
    sketch_table = grouped_scatter(
        (summed * table_scale).reshape(replicas, rows_count, buckets, columns)
    )
    new_momentum = momentum_decay * momentum + sketch_table
    accumulated = error + step_size * new_momentum
    update = (
        jnp.einsum("jbi,jbc->ic", hash_float, accumulated[0], precision=lax.Precision.HIGHEST)
        / rows_count
    )
    encoded = jnp.einsum("jbi,ic->jbc", hash_float, update, precision=lax.Precision.HIGHEST)
    new_error = accumulated - encoded[None]
    return (grad_hidden, update, new_momentum, new_error)


def solution(mesh):
    return jax.shard_map(
        on_device,
        mesh=mesh,
        in_specs=(
            P(("rep", "fsdp"), None),
            P(("rep", "fsdp"), None),
            P("fsdp", None),
            P(None, None, "fsdp"),
            P("fsdp", None, None, "rep"),
            P("fsdp", None, None, "rep"),
        ),
        out_specs=(
            P(("rep", "fsdp"), None),
            P("fsdp", "rep"),
            P("fsdp", None, None, "rep"),
            P("fsdp", None, None, "rep"),
        ),
        check_vma=False,
    )
```

```python
import math

import jax
import jax.numpy as jnp
from jax import lax
from jax.sharding import PartitionSpec as P

momentum_decay = 0.9
step_size = 0.5


def split3(x):
    hi = lax.reduce_precision(x, exponent_bits=8, mantissa_bits=7)
    r1 = x - hi
    mid = lax.reduce_precision(r1, exponent_bits=8, mantissa_bits=7)
    lo = r1 - mid
    return jnp.stack([hi, mid, lo]).astype(jnp.bfloat16)


def grouped_scatter(blocks):
    me = lax.axis_index("rep")
    replicas = blocks.shape[0]
    inner = 4
    outer = replicas // inner
    rest = blocks.shape[1:]
    data = blocks.reshape((outer, inner) + rest)
    low = me % inner
    kept = lax.dynamic_index_in_dim(data, low, axis=1, keepdims=False)
    for mask in range(1, inner):
        send = lax.dynamic_index_in_dim(data, low ^ mask, axis=1, keepdims=False)
        kept = kept + lax.ppermute(send, "rep", [(j, j ^ mask) for j in range(replicas)])
    high = me // inner
    total = lax.dynamic_index_in_dim(kept, high, axis=0, keepdims=False)
    for mask in range(1, outer):
        send = lax.dynamic_index_in_dim(kept, high ^ mask, axis=0, keepdims=False)
        total = total + lax.ppermute(send, "rep", [(j, j ^ (mask * inner)) for j in range(replicas)])
    return total[None]


def on_device(hidden, grad_out, down_weight, hash_tiles, momentum, error):
    shards = lax.axis_size("fsdp")
    replicas = lax.axis_size("rep")
    tok_rows = grad_out.shape[0]
    model_width = grad_out.shape[1]
    shard_rows = down_weight.shape[0]
    rows_count = hash_tiles.shape[0]
    buckets = hash_tiles.shape[1]
    sketch_rows = rows_count * buckets
    columns = model_width // replicas
    total_tokens = tok_rows * shards * replicas
    table_scale = math.sqrt(buckets / (shard_rows * total_tokens))

    hash_float = hash_tiles.astype(jnp.float32)

    hidden_rows = tok_rows * shard_rows // model_width
    outgoing = jnp.concatenate(
        [
            jnp.broadcast_to(grad_out[None], (shards, tok_rows, model_width)),
            hidden.reshape(tok_rows, shards, shard_rows).transpose(1, 0, 2)
            .reshape(shards, hidden_rows, model_width),
        ],
        axis=1,
    )
    arrived = lax.all_to_all(outgoing, "fsdp", split_axis=0, concat_axis=0, tiled=True)
    gathered = arrived[:, :tok_rows]
    hidden_cols = arrived[:, tok_rows:].reshape(shards, tok_rows, shard_rows)
    partial_grads = jnp.einsum(
        "ptd,hd->pth", gathered, down_weight, preferred_element_type=jnp.float32
    ).astype(jnp.bfloat16)
    grad_hidden = lax.all_to_all(
        partial_grads.reshape(shards * tok_rows, shard_rows), "fsdp",
        split_axis=0, concat_axis=1, tiled=True,
    )

    projected = jnp.einsum(
        "ki,pti->kpt",
        hash_tiles.reshape(sketch_rows, shard_rows),
        hidden_cols,
        preferred_element_type=jnp.float32,
    ).reshape(sketch_rows, shards * tok_rows)
    pieces = split3(projected).reshape(3 * sketch_rows, shards * tok_rows)
    products = jnp.einsum(
        "mpt,ptd->md",
        pieces.reshape(3 * sketch_rows, shards, tok_rows),
        gathered,
        preferred_element_type=jnp.float32,
    ).reshape(3, sketch_rows, replicas, columns)
    summed = (products[0] + products[1] + products[2]).transpose(1, 0, 2)
    sketch_table = grouped_scatter(
        (summed * table_scale).reshape(replicas, rows_count, buckets, columns)
    )
    new_momentum = momentum_decay * momentum + sketch_table
    accumulated = error + step_size * new_momentum
    update = (
        jnp.einsum("jbi,jbc->ic", hash_float, accumulated[0], precision=lax.Precision.HIGHEST)
        / rows_count
    )
    encoded = jnp.einsum("jbi,ic->jbc", hash_float, update, precision=lax.Precision.HIGHEST)
    new_error = accumulated - encoded[None]
    return (grad_hidden, update, new_momentum, new_error)


def solution(mesh):
    return jax.shard_map(
        on_device,
        mesh=mesh,
        in_specs=(
            P(("rep", "fsdp"), None),
            P(("rep", "fsdp"), None),
            P("fsdp", None),
            P(None, None, "fsdp"),
            P("fsdp", None, None, "rep"),
            P("fsdp", None, None, "rep"),
        ),
        out_specs=(
            P(("rep", "fsdp"), None),
            P("fsdp", "rep"),
            P("fsdp", None, None, "rep"),
            P("fsdp", None, None, "rep"),
        ),
        check_vma=False,
    )
```

```python
import math

import jax
import jax.numpy as jnp
from jax import lax
from jax.sharding import PartitionSpec as P

momentum_decay = 0.9
step_size = 0.5


def split3(x):
    hi = lax.reduce_precision(x, exponent_bits=8, mantissa_bits=7)
    r1 = x - hi
    mid = lax.reduce_precision(r1, exponent_bits=8, mantissa_bits=7)
    lo = r1 - mid
    return jnp.stack([hi, mid, lo]).astype(jnp.bfloat16)


def grouped_scatter(blocks):
    me = lax.axis_index("rep")
    replicas = blocks.shape[0]
    inner = 4
    outer = replicas // inner
    rest = blocks.shape[1:]
    data = blocks.reshape((outer, inner) + rest)
    low = me % inner
    kept = lax.dynamic_index_in_dim(data, low, axis=1, keepdims=False)
    for mask in range(1, inner):
        send = lax.dynamic_index_in_dim(data, low ^ mask, axis=1, keepdims=False)
        kept = kept + lax.ppermute(send, "rep", [(j, j ^ mask) for j in range(replicas)])
    high = me // inner
    total = lax.dynamic_index_in_dim(kept, high, axis=0, keepdims=False)
    for mask in range(1, outer):
        send = lax.dynamic_index_in_dim(kept, high ^ mask, axis=0, keepdims=False)
        total = total + lax.ppermute(send, "rep", [(j, j ^ (mask * inner)) for j in range(replicas)])
    return total[None]


def on_device(hidden, grad_out, down_weight, hash_tiles, momentum, error):
    shards = lax.axis_size("fsdp")
    replicas = lax.axis_size("rep")
    tok_rows = grad_out.shape[0]
    model_width = grad_out.shape[1]
    shard_rows = down_weight.shape[0]
    rows_count = hash_tiles.shape[0]
    buckets = hash_tiles.shape[1]
    sketch_rows = rows_count * buckets
    columns = model_width // replicas
    total_tokens = tok_rows * shards * replicas
    table_scale = math.sqrt(buckets / (shard_rows * total_tokens))

    hash_float = hash_tiles.astype(jnp.float32)

    outgoing = jnp.concatenate(
        [
            jnp.broadcast_to(grad_out[None], (shards, tok_rows, model_width)),
            hidden.reshape(tok_rows, shards, shard_rows).transpose(1, 0, 2),
        ],
        axis=2,
    )
    arrived = lax.all_to_all(outgoing, "fsdp", split_axis=0, concat_axis=0, tiled=True)
    gathered = arrived[:, :, :model_width]
    hidden_cols = arrived[:, :, model_width:]
    partial_grads = jnp.einsum(
        "ptd,hd->tph", gathered, down_weight, preferred_element_type=jnp.float32
    ).astype(jnp.bfloat16)
    grad_hidden = lax.all_to_all(
        partial_grads, "fsdp", split_axis=1, concat_axis=1, tiled=True
    ).reshape(tok_rows, shards * shard_rows)

    projected = jnp.einsum(
        "ki,pti->kpt",
        hash_tiles.reshape(sketch_rows, shard_rows),
        hidden_cols,
        preferred_element_type=jnp.float32,
    ).reshape(sketch_rows, shards * tok_rows)
    pieces = split3(projected).reshape(3 * sketch_rows, shards * tok_rows)
    products = jnp.einsum(
        "mpt,ptd->md",
        pieces.reshape(3 * sketch_rows, shards, tok_rows),
        gathered,
        preferred_element_type=jnp.float32,
    ).reshape(3, sketch_rows, replicas, columns)
    summed = (products[0] + products[1] + products[2]).transpose(1, 0, 2)
    sketch_table = grouped_scatter(
        (summed * table_scale).reshape(replicas, rows_count, buckets, columns)
    )
    new_momentum = momentum_decay * momentum + sketch_table
    accumulated = error + step_size * new_momentum
    update = (
        jnp.einsum("jbi,jbc->ic", hash_float, accumulated[0], precision=lax.Precision.HIGHEST)
        / rows_count
    )
    encoded = jnp.einsum("jbi,ic->jbc", hash_float, update, precision=lax.Precision.HIGHEST)
    new_error = accumulated - encoded[None]
    return (grad_hidden, update, new_momentum, new_error)


def solution(mesh):
    return jax.shard_map(
        on_device,
        mesh=mesh,
        in_specs=(
            P(("rep", "fsdp"), None),
            P(("rep", "fsdp"), None),
            P("fsdp", None),
            P(None, None, "fsdp"),
            P("fsdp", None, None, "rep"),
            P("fsdp", None, None, "rep"),
        ),
        out_specs=(
            P(("rep", "fsdp"), None),
            P("fsdp", "rep"),
            P("fsdp", None, None, "rep"),
            P("fsdp", None, None, "rep"),
        ),
        check_vma=False,
    )
```

```python
import math

import jax
import jax.numpy as jnp
from jax import lax
from jax.sharding import PartitionSpec as P

momentum_decay = 0.9
step_size = 0.5


def split3(x):
    hi = lax.reduce_precision(x, exponent_bits=8, mantissa_bits=7)
    r1 = x - hi
    mid = lax.reduce_precision(r1, exponent_bits=8, mantissa_bits=7)
    lo = r1 - mid
    return jnp.stack([hi, mid, lo]).astype(jnp.bfloat16)


def grouped_scatter(blocks):
    me = lax.axis_index("rep")
    replicas = blocks.shape[0]
    inner = 4
    outer = replicas // inner
    rest = blocks.shape[1:]
    data = blocks.reshape((outer, inner) + rest)
    low = me % inner
    kept = lax.dynamic_index_in_dim(data, low, axis=1, keepdims=False)
    for mask in range(1, inner):
        send = lax.dynamic_index_in_dim(data, low ^ mask, axis=1, keepdims=False)
        kept = kept + lax.ppermute(send, "rep", [(j, j ^ mask) for j in range(replicas)])
    high = me // inner
    total = lax.dynamic_index_in_dim(kept, high, axis=0, keepdims=False)
    for mask in range(1, outer):
        send = lax.dynamic_index_in_dim(kept, high ^ mask, axis=0, keepdims=False)
        total = total + lax.ppermute(send, "rep", [(j, j ^ (mask * inner)) for j in range(replicas)])
    return total[None]


def on_device(hidden, grad_out, down_weight, hash_tiles, momentum, error):
    shards = lax.axis_size("fsdp")
    replicas = lax.axis_size("rep")
    tok_rows = grad_out.shape[0]
    model_width = grad_out.shape[1]
    shard_rows = down_weight.shape[0]
    rows_count = hash_tiles.shape[0]
    buckets = hash_tiles.shape[1]
    sketch_rows = rows_count * buckets
    columns = model_width // replicas
    total_tokens = tok_rows * shards * replicas
    table_scale = math.sqrt(buckets / (shard_rows * total_tokens))

    hash_float = hash_tiles.astype(jnp.float32)

    outgoing = jnp.concatenate(
        [
            jnp.broadcast_to(grad_out[None], (shards, tok_rows, model_width)),
            hidden.reshape(tok_rows, shards, shard_rows).transpose(1, 0, 2),
        ],
        axis=2,
    )
    arrived = lax.all_to_all(outgoing, "fsdp", split_axis=0, concat_axis=0, tiled=True)
    gathered = arrived[:, :, :model_width]
    hidden_cols = arrived[:, :, model_width:]
    partial_grads = jnp.einsum(
        "ptd,hd->tph", gathered, down_weight, preferred_element_type=jnp.float32
    ).astype(jnp.bfloat16)
    grad_hidden = lax.all_to_all(
        partial_grads, "fsdp", split_axis=1, concat_axis=1, tiled=True
    ).reshape(tok_rows, shards * shard_rows)

    partial_grads, arrived = lax.optimization_barrier((partial_grads, arrived))
    gathered = arrived[:, :, :model_width]
    hidden_cols = arrived[:, :, model_width:]
    projected = jnp.einsum(
        "ki,pti->kpt",
        hash_tiles.reshape(sketch_rows, shard_rows),
        hidden_cols,
        preferred_element_type=jnp.float32,
    ).reshape(sketch_rows, shards * tok_rows)
    pieces = split3(projected).reshape(3 * sketch_rows, shards * tok_rows)
    products = jnp.einsum(
        "mpt,ptd->md",
        pieces.reshape(3 * sketch_rows, shards, tok_rows),
        gathered,
        preferred_element_type=jnp.float32,
    ).reshape(3, sketch_rows, replicas, columns)
    summed = (products[0] + products[1] + products[2]).transpose(1, 0, 2)
    sketch_table = grouped_scatter(
        (summed * table_scale).reshape(replicas, rows_count, buckets, columns)
    )
    new_momentum = momentum_decay * momentum + sketch_table
    accumulated = error + step_size * new_momentum
    update = (
        jnp.einsum("jbi,jbc->ic", hash_float, accumulated[0], precision=lax.Precision.HIGHEST)
        / rows_count
    )
    encoded = jnp.einsum("jbi,ic->jbc", hash_float, update, precision=lax.Precision.HIGHEST)
    new_error = accumulated - encoded[None]
    return (grad_hidden, update, new_momentum, new_error)


def solution(mesh):
    return jax.shard_map(
        on_device,
        mesh=mesh,
        in_specs=(
            P(("rep", "fsdp"), None),
            P(("rep", "fsdp"), None),
            P("fsdp", None),
            P(None, None, "fsdp"),
            P("fsdp", None, None, "rep"),
            P("fsdp", None, None, "rep"),
        ),
        out_specs=(
            P(("rep", "fsdp"), None),
            P("fsdp", "rep"),
            P("fsdp", None, None, "rep"),
            P("fsdp", None, None, "rep"),
        ),
        check_vma=False,
    )
```

```python
import math

import jax
import jax.numpy as jnp
from jax import lax
from jax.sharding import PartitionSpec as P

momentum_decay = 0.9
step_size = 0.5


def split3(x):
    hi = lax.reduce_precision(x, exponent_bits=8, mantissa_bits=7)
    r1 = x - hi
    mid = lax.reduce_precision(r1, exponent_bits=8, mantissa_bits=7)
    lo = r1 - mid
    return jnp.stack([hi, mid, lo]).astype(jnp.bfloat16)


def grouped_scatter(blocks):
    me = lax.axis_index("rep")
    replicas = blocks.shape[0]
    inner = 4
    outer = replicas // inner
    rest = blocks.shape[1:]
    data = blocks.reshape((outer, inner) + rest)
    high = me // inner
    kept = lax.dynamic_index_in_dim(data, high, axis=0, keepdims=False)
    for mask in range(1, outer):
        send = lax.dynamic_index_in_dim(data, high ^ mask, axis=0, keepdims=False)
        kept = kept + lax.ppermute(send, "rep", [(j, j ^ (mask * inner)) for j in range(replicas)])
    low = me % inner
    total = lax.dynamic_index_in_dim(kept, low, axis=0, keepdims=False)
    for mask in range(1, inner):
        send = lax.dynamic_index_in_dim(kept, low ^ mask, axis=0, keepdims=False)
        total = total + lax.ppermute(send, "rep", [(j, j ^ mask) for j in range(replicas)])
    return total[None]


def on_device(hidden, grad_out, down_weight, hash_tiles, momentum, error):
    shards = lax.axis_size("fsdp")
    replicas = lax.axis_size("rep")
    tok_rows = grad_out.shape[0]
    model_width = grad_out.shape[1]
    shard_rows = down_weight.shape[0]
    rows_count = hash_tiles.shape[0]
    buckets = hash_tiles.shape[1]
    sketch_rows = rows_count * buckets
    columns = model_width // replicas
    total_tokens = tok_rows * shards * replicas
    table_scale = math.sqrt(buckets / (shard_rows * total_tokens))

    hash_float = hash_tiles.astype(jnp.float32)

    outgoing = jnp.concatenate(
        [
            jnp.broadcast_to(grad_out[None], (shards, tok_rows, model_width)),
            hidden.reshape(tok_rows, shards, shard_rows).transpose(1, 0, 2),
        ],
        axis=2,
    )
    arrived = lax.all_to_all(outgoing, "fsdp", split_axis=0, concat_axis=0, tiled=True)
    gathered = arrived[:, :, :model_width]
    hidden_cols = arrived[:, :, model_width:]
    partial_grads = jnp.einsum(
        "ptd,hd->tph", gathered, down_weight, preferred_element_type=jnp.float32
    ).astype(jnp.bfloat16)
    grad_hidden = lax.all_to_all(
        partial_grads, "fsdp", split_axis=1, concat_axis=1, tiled=True
    ).reshape(tok_rows, shards * shard_rows)

    projected = jnp.einsum(
        "ki,pti->kpt",
        hash_tiles.reshape(sketch_rows, shard_rows),
        hidden_cols,
        preferred_element_type=jnp.float32,
    ).reshape(sketch_rows, shards * tok_rows)
    pieces = split3(projected).reshape(3 * sketch_rows, shards * tok_rows)
    products = jnp.einsum(
        "mpt,ptd->md",
        pieces.reshape(3 * sketch_rows, shards, tok_rows),
        gathered,
        preferred_element_type=jnp.float32,
    ).reshape(3, sketch_rows, replicas, columns)
    summed = (products[0] + products[1] + products[2]).transpose(1, 0, 2)
    sketch_table = grouped_scatter(
        (summed * table_scale).reshape(replicas, rows_count, buckets, columns)
    )
    new_momentum = momentum_decay * momentum + sketch_table
    accumulated = error + step_size * new_momentum
    update = (
        jnp.einsum("jbi,jbc->ic", hash_float, accumulated[0], precision=lax.Precision.HIGHEST)
        / rows_count
    )
    encoded = jnp.einsum("jbi,ic->jbc", hash_float, update, precision=lax.Precision.HIGHEST)
    new_error = accumulated - encoded[None]
    return (grad_hidden, update, new_momentum, new_error)


def solution(mesh):
    return jax.shard_map(
        on_device,
        mesh=mesh,
        in_specs=(
            P(("rep", "fsdp"), None),
            P(("rep", "fsdp"), None),
            P("fsdp", None),
            P(None, None, "fsdp"),
            P("fsdp", None, None, "rep"),
            P("fsdp", None, None, "rep"),
        ),
        out_specs=(
            P(("rep", "fsdp"), None),
            P("fsdp", "rep"),
            P("fsdp", None, None, "rep"),
            P("fsdp", None, None, "rep"),
        ),
        check_vma=False,
    )
```

```python
import math

import jax
import jax.numpy as jnp
from jax import lax
from jax.sharding import PartitionSpec as P

momentum_decay = 0.9
step_size = 0.5


def split3(x):
    hi = lax.reduce_precision(x, exponent_bits=8, mantissa_bits=7)
    r1 = x - hi
    mid = lax.reduce_precision(r1, exponent_bits=8, mantissa_bits=7)
    lo = r1 - mid
    return jnp.stack([hi, mid, lo]).astype(jnp.bfloat16)


def grouped_scatter(blocks):
    me = lax.axis_index("rep")
    replicas = blocks.shape[0]
    inner = 4
    outer = replicas // inner
    rest = blocks.shape[1:]
    data = blocks.reshape((outer, inner) + rest)
    low = me % inner
    kept = lax.dynamic_index_in_dim(data, low, axis=1, keepdims=False)
    for mask in range(1, inner):
        send = lax.dynamic_index_in_dim(data, low ^ mask, axis=1, keepdims=False)
        kept = kept + lax.ppermute(send, "rep", [(j, j ^ mask) for j in range(replicas)])
    high = me // inner
    total = lax.dynamic_index_in_dim(kept, high, axis=0, keepdims=False)
    for mask in range(1, outer):
        send = lax.dynamic_index_in_dim(kept, high ^ mask, axis=0, keepdims=False)
        total = total + lax.ppermute(send, "rep", [(j, j ^ (mask * inner)) for j in range(replicas)])
    return total[None]


def on_device(hidden, grad_out, down_weight, hash_tiles, momentum, error):
    shards = lax.axis_size("fsdp")
    replicas = lax.axis_size("rep")
    tok_rows = grad_out.shape[0]
    model_width = grad_out.shape[1]
    shard_rows = down_weight.shape[0]
    rows_count = hash_tiles.shape[0]
    buckets = hash_tiles.shape[1]
    sketch_rows = rows_count * buckets
    columns = model_width // replicas
    total_tokens = tok_rows * shards * replicas
    table_scale = math.sqrt(buckets / (shard_rows * total_tokens))

    hash_float = hash_tiles.astype(jnp.float32)

    outgoing = jnp.concatenate(
        [
            jnp.broadcast_to(grad_out[None], (shards, tok_rows, model_width)),
            jnp.stack([hidden[:, p * shard_rows:(p + 1) * shard_rows] for p in range(shards)]),
        ],
        axis=2,
    )
    arrived = lax.all_to_all(outgoing, "fsdp", split_axis=0, concat_axis=0, tiled=True)
    gathered = arrived[:, :, :model_width]
    hidden_cols = arrived[:, :, model_width:]
    partial_grads = jnp.einsum(
        "ptd,hd->tph", gathered, down_weight, preferred_element_type=jnp.float32
    ).astype(jnp.bfloat16)
    grad_hidden = lax.all_to_all(
        partial_grads, "fsdp", split_axis=1, concat_axis=1, tiled=True
    ).reshape(tok_rows, shards * shard_rows)

    projected = jnp.einsum(
        "ki,pti->kpt",
        hash_tiles.reshape(sketch_rows, shard_rows),
        hidden_cols,
        preferred_element_type=jnp.float32,
    ).reshape(sketch_rows, shards * tok_rows)
    pieces = split3(projected).reshape(3 * sketch_rows, shards * tok_rows)
    products = jnp.einsum(
        "mpt,ptd->md",
        pieces.reshape(3 * sketch_rows, shards, tok_rows),
        gathered,
        preferred_element_type=jnp.float32,
    ).reshape(3, sketch_rows, replicas, columns)
    summed = (products[0] + products[1] + products[2]).transpose(1, 0, 2)
    sketch_table = grouped_scatter(
        (summed * table_scale).reshape(replicas, rows_count, buckets, columns)
    )
    new_momentum = momentum_decay * momentum + sketch_table
    accumulated = error + step_size * new_momentum
    update = (
        jnp.einsum("jbi,jbc->ic", hash_float, accumulated[0], precision=lax.Precision.HIGHEST)
        / rows_count
    )
    encoded = jnp.einsum("jbi,ic->jbc", hash_float, update, precision=lax.Precision.HIGHEST)
    new_error = accumulated - encoded[None]
    return (grad_hidden, update, new_momentum, new_error)


def solution(mesh):
    return jax.shard_map(
        on_device,
        mesh=mesh,
        in_specs=(
            P(("rep", "fsdp"), None),
            P(("rep", "fsdp"), None),
            P("fsdp", None),
            P(None, None, "fsdp"),
            P("fsdp", None, None, "rep"),
            P("fsdp", None, None, "rep"),
        ),
        out_specs=(
            P(("rep", "fsdp"), None),
            P("fsdp", "rep"),
            P("fsdp", None, None, "rep"),
            P("fsdp", None, None, "rep"),
        ),
        check_vma=False,
    )
```

```python
import math

import jax
import jax.numpy as jnp
from jax import lax
from jax.experimental import pallas as pl
from jax.sharding import PartitionSpec as P

momentum_decay = 0.9
step_size = 0.5


def _place_block(block_ref, out_ref):
    out_ref[...] = block_ref[0]


def place_blocks(blocks):
    count, rows, width = blocks.shape
    return pl.pallas_call(
        _place_block,
        out_shape=jax.ShapeDtypeStruct((rows, count * width), blocks.dtype),
        grid=(count,),
        in_specs=[pl.BlockSpec((1, rows, width), lambda i: (i, 0, 0))],
        out_specs=pl.BlockSpec((rows, width), lambda i: (0, i)),
    )(blocks)


def split3(x):
    hi = lax.reduce_precision(x, exponent_bits=8, mantissa_bits=7)
    r1 = x - hi
    mid = lax.reduce_precision(r1, exponent_bits=8, mantissa_bits=7)
    lo = r1 - mid
    return jnp.stack([hi, mid, lo]).astype(jnp.bfloat16)


def grouped_scatter(blocks):
    me = lax.axis_index("rep")
    replicas = blocks.shape[0]
    inner = 4
    outer = replicas // inner
    rest = blocks.shape[1:]
    data = blocks.reshape((outer, inner) + rest)
    low = me % inner
    kept = lax.dynamic_index_in_dim(data, low, axis=1, keepdims=False)
    for mask in range(1, inner):
        send = lax.dynamic_index_in_dim(data, low ^ mask, axis=1, keepdims=False)
        kept = kept + lax.ppermute(send, "rep", [(j, j ^ mask) for j in range(replicas)])
    high = me // inner
    total = lax.dynamic_index_in_dim(kept, high, axis=0, keepdims=False)
    for mask in range(1, outer):
        send = lax.dynamic_index_in_dim(kept, high ^ mask, axis=0, keepdims=False)
        total = total + lax.ppermute(send, "rep", [(j, j ^ (mask * inner)) for j in range(replicas)])
    return total[None]


def on_device(hidden, grad_out, down_weight, hash_tiles, momentum, error):
    shards = lax.axis_size("fsdp")
    replicas = lax.axis_size("rep")
    tok_rows = grad_out.shape[0]
    model_width = grad_out.shape[1]
    shard_rows = down_weight.shape[0]
    rows_count = hash_tiles.shape[0]
    buckets = hash_tiles.shape[1]
    sketch_rows = rows_count * buckets
    columns = model_width // replicas
    total_tokens = tok_rows * shards * replicas
    table_scale = math.sqrt(buckets / (shard_rows * total_tokens))

    hash_float = hash_tiles.astype(jnp.float32)

    outgoing = jnp.concatenate(
        [
            jnp.broadcast_to(grad_out[None], (shards, tok_rows, model_width)),
            hidden.reshape(tok_rows, shards, shard_rows).transpose(1, 0, 2),
        ],
        axis=2,
    )
    arrived = lax.all_to_all(outgoing, "fsdp", split_axis=0, concat_axis=0, tiled=True)
    gathered = arrived[:, :, :model_width]
    hidden_cols = arrived[:, :, model_width:]
    partial_grads = jnp.einsum(
        "ptd,hd->pth", gathered, down_weight, preferred_element_type=jnp.float32
    ).astype(jnp.bfloat16)
    grad_hidden = place_blocks(
        lax.all_to_all(partial_grads, "fsdp", split_axis=0, concat_axis=0, tiled=True)
    )

    projected = jnp.einsum(
        "ki,pti->kpt",
        hash_tiles.reshape(sketch_rows, shard_rows),
        hidden_cols,
        preferred_element_type=jnp.float32,
    ).reshape(sketch_rows, shards * tok_rows)
    pieces = split3(projected).reshape(3 * sketch_rows, shards * tok_rows)
    products = jnp.einsum(
        "mpt,ptd->md",
        pieces.reshape(3 * sketch_rows, shards, tok_rows),
        gathered,
        preferred_element_type=jnp.float32,
    ).reshape(3, sketch_rows, replicas, columns)
    summed = (products[0] + products[1] + products[2]).transpose(1, 0, 2)
    sketch_table = grouped_scatter(
        (summed * table_scale).reshape(replicas, rows_count, buckets, columns)
    )
    new_momentum = momentum_decay * momentum + sketch_table
    accumulated = error + step_size * new_momentum
    update = (
        jnp.einsum("jbi,jbc->ic", hash_float, accumulated[0], precision=lax.Precision.HIGHEST)
        / rows_count
    )
    encoded = jnp.einsum("jbi,ic->jbc", hash_float, update, precision=lax.Precision.HIGHEST)
    new_error = accumulated - encoded[None]
    return (grad_hidden, update, new_momentum, new_error)


def solution(mesh):
    return jax.shard_map(
        on_device,
        mesh=mesh,
        in_specs=(
            P(("rep", "fsdp"), None),
            P(("rep", "fsdp"), None),
            P("fsdp", None),
            P(None, None, "fsdp"),
            P("fsdp", None, None, "rep"),
            P("fsdp", None, None, "rep"),
        ),
        out_specs=(
            P(("rep", "fsdp"), None),
            P("fsdp", "rep"),
            P("fsdp", None, None, "rep"),
            P("fsdp", None, None, "rep"),
        ),
        check_vma=False,
    )
```

```python
import math

import jax
import jax.numpy as jnp
from jax import lax
from jax.experimental import pallas as pl
from jax.experimental.pallas import tpu as pltpu
from jax.sharding import PartitionSpec as P

momentum_decay = 0.9
step_size = 0.5


def place_blocks(blocks):
    count, rows, width = blocks.shape

    def body(block_ref, out_ref):
        for p in range(count):
            out_ref[:, p * width:(p + 1) * width] = block_ref[p]

    return pl.pallas_call(
        body,
        out_shape=jax.ShapeDtypeStruct((rows, count * width), blocks.dtype),
        in_specs=[pl.BlockSpec(memory_space=pltpu.VMEM)],
        out_specs=pl.BlockSpec(memory_space=pltpu.VMEM),
    )(blocks)


def split3(x):
    hi = lax.reduce_precision(x, exponent_bits=8, mantissa_bits=7)
    r1 = x - hi
    mid = lax.reduce_precision(r1, exponent_bits=8, mantissa_bits=7)
    lo = r1 - mid
    return jnp.stack([hi, mid, lo]).astype(jnp.bfloat16)


def grouped_scatter(blocks):
    me = lax.axis_index("rep")
    replicas = blocks.shape[0]
    inner = 4
    outer = replicas // inner
    rest = blocks.shape[1:]
    data = blocks.reshape((outer, inner) + rest)
    low = me % inner
    kept = lax.dynamic_index_in_dim(data, low, axis=1, keepdims=False)
    for mask in range(1, inner):
        send = lax.dynamic_index_in_dim(data, low ^ mask, axis=1, keepdims=False)
        kept = kept + lax.ppermute(send, "rep", [(j, j ^ mask) for j in range(replicas)])
    high = me // inner
    total = lax.dynamic_index_in_dim(kept, high, axis=0, keepdims=False)
    for mask in range(1, outer):
        send = lax.dynamic_index_in_dim(kept, high ^ mask, axis=0, keepdims=False)
        total = total + lax.ppermute(send, "rep", [(j, j ^ (mask * inner)) for j in range(replicas)])
    return total[None]


def on_device(hidden, grad_out, down_weight, hash_tiles, momentum, error):
    shards = lax.axis_size("fsdp")
    replicas = lax.axis_size("rep")
    tok_rows = grad_out.shape[0]
    model_width = grad_out.shape[1]
    shard_rows = down_weight.shape[0]
    rows_count = hash_tiles.shape[0]
    buckets = hash_tiles.shape[1]
    sketch_rows = rows_count * buckets
    columns = model_width // replicas
    total_tokens = tok_rows * shards * replicas
    table_scale = math.sqrt(buckets / (shard_rows * total_tokens))

    hash_float = hash_tiles.astype(jnp.float32)

    outgoing = jnp.concatenate(
        [
            jnp.broadcast_to(grad_out[None], (shards, tok_rows, model_width)),
            hidden.reshape(tok_rows, shards, shard_rows).transpose(1, 0, 2),
        ],
        axis=2,
    )
    arrived = lax.all_to_all(outgoing, "fsdp", split_axis=0, concat_axis=0, tiled=True)
    gathered = arrived[:, :, :model_width]
    hidden_cols = arrived[:, :, model_width:]
    partial_grads = jnp.einsum(
        "ptd,hd->pth", gathered, down_weight, preferred_element_type=jnp.float32
    ).astype(jnp.bfloat16)
    grad_hidden = place_blocks(
        lax.all_to_all(partial_grads, "fsdp", split_axis=0, concat_axis=0, tiled=True)
    )

    projected = jnp.einsum(
        "ki,pti->kpt",
        hash_tiles.reshape(sketch_rows, shard_rows),
        hidden_cols,
        preferred_element_type=jnp.float32,
    ).reshape(sketch_rows, shards * tok_rows)
    pieces = split3(projected).reshape(3 * sketch_rows, shards * tok_rows)
    products = jnp.einsum(
        "mpt,ptd->md",
        pieces.reshape(3 * sketch_rows, shards, tok_rows),
        gathered,
        preferred_element_type=jnp.float32,
    ).reshape(3, sketch_rows, replicas, columns)
    summed = (products[0] + products[1] + products[2]).transpose(1, 0, 2)
    sketch_table = grouped_scatter(
        (summed * table_scale).reshape(replicas, rows_count, buckets, columns)
    )
    new_momentum = momentum_decay * momentum + sketch_table
    accumulated = error + step_size * new_momentum
    update = (
        jnp.einsum("jbi,jbc->ic", hash_float, accumulated[0], precision=lax.Precision.HIGHEST)
        / rows_count
    )
    encoded = jnp.einsum("jbi,ic->jbc", hash_float, update, precision=lax.Precision.HIGHEST)
    new_error = accumulated - encoded[None]
    return (grad_hidden, update, new_momentum, new_error)


def solution(mesh):
    return jax.shard_map(
        on_device,
        mesh=mesh,
        in_specs=(
            P(("rep", "fsdp"), None),
            P(("rep", "fsdp"), None),
            P("fsdp", None),
            P(None, None, "fsdp"),
            P("fsdp", None, None, "rep"),
            P("fsdp", None, None, "rep"),
        ),
        out_specs=(
            P(("rep", "fsdp"), None),
            P("fsdp", "rep"),
            P("fsdp", None, None, "rep"),
            P("fsdp", None, None, "rep"),
        ),
        check_vma=False,
    )
```

```python
import math

import jax
import jax.numpy as jnp
from jax import lax
from jax.experimental import pallas as pl
from jax.experimental.pallas import tpu as pltpu
from jax.sharding import PartitionSpec as P

momentum_decay = 0.9
step_size = 0.5


def place_blocks(blocks):
    count, rows, width = blocks.shape

    def body(block_ref, out_ref):
        for p in range(count):
            out_ref[:, p * width:(p + 1) * width] = block_ref[p]

    return pl.pallas_call(
        body,
        out_shape=jax.ShapeDtypeStruct((rows, count * width), blocks.dtype),
        in_specs=[pl.BlockSpec(memory_space=pltpu.VMEM)],
        out_specs=pl.BlockSpec(memory_space=pltpu.VMEM),
    )(blocks)


def build_outgoing(grad_out, hidden, count):
    rows, width = grad_out.shape
    block = hidden.shape[1] // count

    def body(grad_ref, hidden_ref, out_ref):
        for p in range(count):
            out_ref[p, :, :width] = grad_ref[...]
            out_ref[p, :, width:] = hidden_ref[:, p * block:(p + 1) * block]

    return pl.pallas_call(
        body,
        out_shape=jax.ShapeDtypeStruct((count, rows, width + block), grad_out.dtype),
        in_specs=[pl.BlockSpec(memory_space=pltpu.VMEM)] * 2,
        out_specs=pl.BlockSpec(memory_space=pltpu.VMEM),
    )(grad_out, hidden)


def split3(x):
    hi = lax.reduce_precision(x, exponent_bits=8, mantissa_bits=7)
    r1 = x - hi
    mid = lax.reduce_precision(r1, exponent_bits=8, mantissa_bits=7)
    lo = r1 - mid
    return jnp.stack([hi, mid, lo]).astype(jnp.bfloat16)


def grouped_scatter(blocks):
    me = lax.axis_index("rep")
    replicas = blocks.shape[0]
    inner = 4
    outer = replicas // inner
    rest = blocks.shape[1:]
    data = blocks.reshape((outer, inner) + rest)
    low = me % inner
    kept = lax.dynamic_index_in_dim(data, low, axis=1, keepdims=False)
    for mask in range(1, inner):
        send = lax.dynamic_index_in_dim(data, low ^ mask, axis=1, keepdims=False)
        kept = kept + lax.ppermute(send, "rep", [(j, j ^ mask) for j in range(replicas)])
    high = me // inner
    total = lax.dynamic_index_in_dim(kept, high, axis=0, keepdims=False)
    for mask in range(1, outer):
        send = lax.dynamic_index_in_dim(kept, high ^ mask, axis=0, keepdims=False)
        total = total + lax.ppermute(send, "rep", [(j, j ^ (mask * inner)) for j in range(replicas)])
    return total[None]


def on_device(hidden, grad_out, down_weight, hash_tiles, momentum, error):
    shards = lax.axis_size("fsdp")
    replicas = lax.axis_size("rep")
    tok_rows = grad_out.shape[0]
    model_width = grad_out.shape[1]
    shard_rows = down_weight.shape[0]
    rows_count = hash_tiles.shape[0]
    buckets = hash_tiles.shape[1]
    sketch_rows = rows_count * buckets
    columns = model_width // replicas
    total_tokens = tok_rows * shards * replicas
    table_scale = math.sqrt(buckets / (shard_rows * total_tokens))

    hash_float = hash_tiles.astype(jnp.float32)

    outgoing = build_outgoing(grad_out, hidden, shards)
    arrived = lax.all_to_all(outgoing, "fsdp", split_axis=0, concat_axis=0, tiled=True)
    gathered = arrived[:, :, :model_width]
    hidden_cols = arrived[:, :, model_width:]
    partial_grads = jnp.einsum(
        "ptd,hd->pth", gathered, down_weight, preferred_element_type=jnp.float32
    ).astype(jnp.bfloat16)
    grad_hidden = place_blocks(
        lax.all_to_all(partial_grads, "fsdp", split_axis=0, concat_axis=0, tiled=True)
    )

    projected = jnp.einsum(
        "ki,pti->kpt",
        hash_tiles.reshape(sketch_rows, shard_rows),
        hidden_cols,
        preferred_element_type=jnp.float32,
    ).reshape(sketch_rows, shards * tok_rows)
    pieces = split3(projected).reshape(3 * sketch_rows, shards * tok_rows)
    products = jnp.einsum(
        "mpt,ptd->md",
        pieces.reshape(3 * sketch_rows, shards, tok_rows),
        gathered,
        preferred_element_type=jnp.float32,
    ).reshape(3, sketch_rows, replicas, columns)
    summed = (products[0] + products[1] + products[2]).transpose(1, 0, 2)
    sketch_table = grouped_scatter(
        (summed * table_scale).reshape(replicas, rows_count, buckets, columns)
    )
    new_momentum = momentum_decay * momentum + sketch_table
    accumulated = error + step_size * new_momentum
    update = (
        jnp.einsum("jbi,jbc->ic", hash_float, accumulated[0], precision=lax.Precision.HIGHEST)
        / rows_count
    )
    encoded = jnp.einsum("jbi,ic->jbc", hash_float, update, precision=lax.Precision.HIGHEST)
    new_error = accumulated - encoded[None]
    return (grad_hidden, update, new_momentum, new_error)


def solution(mesh):
    return jax.shard_map(
        on_device,
        mesh=mesh,
        in_specs=(
            P(("rep", "fsdp"), None),
            P(("rep", "fsdp"), None),
            P("fsdp", None),
            P(None, None, "fsdp"),
            P("fsdp", None, None, "rep"),
            P("fsdp", None, None, "rep"),
        ),
        out_specs=(
            P(("rep", "fsdp"), None),
            P("fsdp", "rep"),
            P("fsdp", None, None, "rep"),
            P("fsdp", None, None, "rep"),
        ),
        check_vma=False,
    )
```

```python
import math

import jax
import jax.numpy as jnp
from jax import lax
from jax.experimental import pallas as pl
from jax.experimental.pallas import tpu as pltpu
from jax.sharding import PartitionSpec as P

momentum_decay = 0.9
step_size = 0.5


def place_blocks(blocks):
    count, rows, width = blocks.shape

    def body(block_ref, out_ref, sems):
        copies = [
            pltpu.make_async_copy(
                block_ref.at[p], out_ref.at[:, pl.ds(p * width, width)], sems.at[p]
            )
            for p in range(count)
        ]
        for c in copies:
            c.start()
        for c in copies:
            c.wait()

    return pl.pallas_call(
        body,
        out_shape=jax.ShapeDtypeStruct((rows, count * width), blocks.dtype),
        in_specs=[pl.BlockSpec(memory_space=pl.ANY)],
        out_specs=pl.BlockSpec(memory_space=pl.ANY),
        scratch_shapes=[pltpu.SemaphoreType.DMA((count,))],
    )(blocks)


def build_outgoing(grad_out, hidden, count):
    rows, width = grad_out.shape
    block = hidden.shape[1] // count

    def body(grad_ref, hidden_ref, out_ref):
        for p in range(count):
            out_ref[p, :, :width] = grad_ref[...]
            out_ref[p, :, width:] = hidden_ref[:, p * block:(p + 1) * block]

    return pl.pallas_call(
        body,
        out_shape=jax.ShapeDtypeStruct((count, rows, width + block), grad_out.dtype),
        in_specs=[pl.BlockSpec(memory_space=pltpu.VMEM)] * 2,
        out_specs=pl.BlockSpec(memory_space=pltpu.VMEM),
    )(grad_out, hidden)


def split3(x):
    hi = lax.reduce_precision(x, exponent_bits=8, mantissa_bits=7)
    r1 = x - hi
    mid = lax.reduce_precision(r1, exponent_bits=8, mantissa_bits=7)
    lo = r1 - mid
    return jnp.stack([hi, mid, lo]).astype(jnp.bfloat16)


def grouped_scatter(blocks):
    me = lax.axis_index("rep")
    replicas = blocks.shape[0]
    inner = 4
    outer = replicas // inner
    rest = blocks.shape[1:]
    data = blocks.reshape((outer, inner) + rest)
    low = me % inner
    kept = lax.dynamic_index_in_dim(data, low, axis=1, keepdims=False)
    for mask in range(1, inner):
        send = lax.dynamic_index_in_dim(data, low ^ mask, axis=1, keepdims=False)
        kept = kept + lax.ppermute(send, "rep", [(j, j ^ mask) for j in range(replicas)])
    high = me // inner
    total = lax.dynamic_index_in_dim(kept, high, axis=0, keepdims=False)
    for mask in range(1, outer):
        send = lax.dynamic_index_in_dim(kept, high ^ mask, axis=0, keepdims=False)
        total = total + lax.ppermute(send, "rep", [(j, j ^ (mask * inner)) for j in range(replicas)])
    return total[None]


def on_device(hidden, grad_out, down_weight, hash_tiles, momentum, error):
    shards = lax.axis_size("fsdp")
    replicas = lax.axis_size("rep")
    tok_rows = grad_out.shape[0]
    model_width = grad_out.shape[1]
    shard_rows = down_weight.shape[0]
    rows_count = hash_tiles.shape[0]
    buckets = hash_tiles.shape[1]
    sketch_rows = rows_count * buckets
    columns = model_width // replicas
    total_tokens = tok_rows * shards * replicas
    table_scale = math.sqrt(buckets / (shard_rows * total_tokens))

    hash_float = hash_tiles.astype(jnp.float32)

    outgoing = build_outgoing(grad_out, hidden, shards)
    arrived = lax.all_to_all(outgoing, "fsdp", split_axis=0, concat_axis=0, tiled=True)
    gathered = arrived[:, :, :model_width]
    hidden_cols = arrived[:, :, model_width:]
    partial_grads = jnp.einsum(
        "ptd,hd->pth", gathered, down_weight, preferred_element_type=jnp.float32
    ).astype(jnp.bfloat16)
    grad_hidden = place_blocks(
        lax.all_to_all(partial_grads, "fsdp", split_axis=0, concat_axis=0, tiled=True)
    )

    projected = jnp.einsum(
        "ki,pti->kpt",
        hash_tiles.reshape(sketch_rows, shard_rows),
        hidden_cols,
        preferred_element_type=jnp.float32,
    ).reshape(sketch_rows, shards * tok_rows)
    pieces = split3(projected).reshape(3 * sketch_rows, shards * tok_rows)
    products = jnp.einsum(
        "mpt,ptd->md",
        pieces.reshape(3 * sketch_rows, shards, tok_rows),
        gathered,
        preferred_element_type=jnp.float32,
    ).reshape(3, sketch_rows, replicas, columns)
    summed = (products[0] + products[1] + products[2]).transpose(1, 0, 2)
    sketch_table = grouped_scatter(
        (summed * table_scale).reshape(replicas, rows_count, buckets, columns)
    )
    new_momentum = momentum_decay * momentum + sketch_table
    accumulated = error + step_size * new_momentum
    update = (
        jnp.einsum("jbi,jbc->ic", hash_float, accumulated[0], precision=lax.Precision.HIGHEST)
        / rows_count
    )
    encoded = jnp.einsum("jbi,ic->jbc", hash_float, update, precision=lax.Precision.HIGHEST)
    new_error = accumulated - encoded[None]
    return (grad_hidden, update, new_momentum, new_error)


def solution(mesh):
    return jax.shard_map(
        on_device,
        mesh=mesh,
        in_specs=(
            P(("rep", "fsdp"), None),
            P(("rep", "fsdp"), None),
            P("fsdp", None),
            P(None, None, "fsdp"),
            P("fsdp", None, None, "rep"),
            P("fsdp", None, None, "rep"),
        ),
        out_specs=(
            P(("rep", "fsdp"), None),
            P("fsdp", "rep"),
            P("fsdp", None, None, "rep"),
            P("fsdp", None, None, "rep"),
        ),
        check_vma=False,
    )
```

```python
import math

import jax
import jax.numpy as jnp
from jax import lax
from jax.experimental import pallas as pl
from jax.experimental.pallas import tpu as pltpu
from jax.sharding import PartitionSpec as P

momentum_decay = 0.9
step_size = 0.5


def place_blocks(blocks):
    count, rows, width = blocks.shape

    def body(block_ref, out_ref, sems):
        copies = [
            pltpu.make_async_copy(
                block_ref.at[p], out_ref.at[:, pl.ds(p * width, width)], sems.at[p]
            )
            for p in range(count)
        ]
        for c in copies:
            c.start()
        for c in copies:
            c.wait()

    return pl.pallas_call(
        body,
        out_shape=jax.ShapeDtypeStruct((rows, count * width), blocks.dtype),
        in_specs=[pl.BlockSpec(memory_space=pl.ANY)],
        out_specs=pl.BlockSpec(memory_space=pltpu.VMEM),
        scratch_shapes=[pltpu.SemaphoreType.DMA((count,))],
    )(blocks)


def build_outgoing(grad_out, hidden, count):
    rows, width = grad_out.shape
    block = hidden.shape[1] // count

    def body(grad_ref, hidden_ref, out_ref):
        for p in range(count):
            out_ref[p, :, :width] = grad_ref[...]
            out_ref[p, :, width:] = hidden_ref[:, p * block:(p + 1) * block]

    return pl.pallas_call(
        body,
        out_shape=jax.ShapeDtypeStruct((count, rows, width + block), grad_out.dtype),
        in_specs=[pl.BlockSpec(memory_space=pltpu.VMEM)] * 2,
        out_specs=pl.BlockSpec(memory_space=pltpu.VMEM),
    )(grad_out, hidden)


def split3(x):
    hi = lax.reduce_precision(x, exponent_bits=8, mantissa_bits=7)
    r1 = x - hi
    mid = lax.reduce_precision(r1, exponent_bits=8, mantissa_bits=7)
    lo = r1 - mid
    return jnp.stack([hi, mid, lo]).astype(jnp.bfloat16)


def grouped_scatter(blocks):
    me = lax.axis_index("rep")
    replicas = blocks.shape[0]
    inner = 4
    outer = replicas // inner
    rest = blocks.shape[1:]
    data = blocks.reshape((outer, inner) + rest)
    low = me % inner
    kept = lax.dynamic_index_in_dim(data, low, axis=1, keepdims=False)
    for mask in range(1, inner):
        send = lax.dynamic_index_in_dim(data, low ^ mask, axis=1, keepdims=False)
        kept = kept + lax.ppermute(send, "rep", [(j, j ^ mask) for j in range(replicas)])
    high = me // inner
    total = lax.dynamic_index_in_dim(kept, high, axis=0, keepdims=False)
    for mask in range(1, outer):
        send = lax.dynamic_index_in_dim(kept, high ^ mask, axis=0, keepdims=False)
        total = total + lax.ppermute(send, "rep", [(j, j ^ (mask * inner)) for j in range(replicas)])
    return total[None]


def on_device(hidden, grad_out, down_weight, hash_tiles, momentum, error):
    shards = lax.axis_size("fsdp")
    replicas = lax.axis_size("rep")
    tok_rows = grad_out.shape[0]
    model_width = grad_out.shape[1]
    shard_rows = down_weight.shape[0]
    rows_count = hash_tiles.shape[0]
    buckets = hash_tiles.shape[1]
    sketch_rows = rows_count * buckets
    columns = model_width // replicas
    total_tokens = tok_rows * shards * replicas
    table_scale = math.sqrt(buckets / (shard_rows * total_tokens))

    hash_float = hash_tiles.astype(jnp.float32)

    outgoing = build_outgoing(grad_out, hidden, shards)
    arrived = lax.all_to_all(outgoing, "fsdp", split_axis=0, concat_axis=0, tiled=True)
    gathered = arrived[:, :, :model_width]
    hidden_cols = arrived[:, :, model_width:]
    partial_grads = jnp.einsum(
        "ptd,hd->pth", gathered, down_weight, preferred_element_type=jnp.float32
    ).astype(jnp.bfloat16)
    grad_hidden = place_blocks(
        lax.all_to_all(partial_grads, "fsdp", split_axis=0, concat_axis=0, tiled=True)
    )

    projected = jnp.einsum(
        "ki,pti->kpt",
        hash_tiles.reshape(sketch_rows, shard_rows),
        hidden_cols,
        preferred_element_type=jnp.float32,
    ).reshape(sketch_rows, shards * tok_rows)
    pieces = split3(projected).reshape(3 * sketch_rows, shards * tok_rows)
    products = jnp.einsum(
        "mpt,ptd->md",
        pieces.reshape(3 * sketch_rows, shards, tok_rows),
        gathered,
        preferred_element_type=jnp.float32,
    ).reshape(3, sketch_rows, replicas, columns)
    summed = (products[0] + products[1] + products[2]).transpose(1, 0, 2)
    sketch_table = grouped_scatter(
        (summed * table_scale).reshape(replicas, rows_count, buckets, columns)
    )
    new_momentum = momentum_decay * momentum + sketch_table
    accumulated = error + step_size * new_momentum
    update = (
        jnp.einsum("jbi,jbc->ic", hash_float, accumulated[0], precision=lax.Precision.HIGHEST)
        / rows_count
    )
    encoded = jnp.einsum("jbi,ic->jbc", hash_float, update, precision=lax.Precision.HIGHEST)
    new_error = accumulated - encoded[None]
    return (grad_hidden, update, new_momentum, new_error)


def solution(mesh):
    return jax.shard_map(
        on_device,
        mesh=mesh,
        in_specs=(
            P(("rep", "fsdp"), None),
            P(("rep", "fsdp"), None),
            P("fsdp", None),
            P(None, None, "fsdp"),
            P("fsdp", None, None, "rep"),
            P("fsdp", None, None, "rep"),
        ),
        out_specs=(
            P(("rep", "fsdp"), None),
            P("fsdp", "rep"),
            P("fsdp", None, None, "rep"),
            P("fsdp", None, None, "rep"),
        ),
        check_vma=False,
    )
```
